512 devices in a mesh: req: 128 (over z, x, core), head: 4 (over y).
Axes of the slice: x: 4, y: 4, z: 16, core: 2. Of those that a mesh axis runs over, the one named last changes fastest.
Arguments:
- query_proj: bfloat16 [32768, 2048], P('req', 'head'), may hold values from -6 to 6
- key_proj: bfloat16 [32768, 2048], P('req', 'head'), may hold values from -6 to 6
- value_proj: bfloat16 [32768, 2048], P('req', 'head'), may hold values from -6 to 6
- lengths: int32 [64], replicated, may hold values from 1 to 8, 256 in all
- page_table: int32 [256], P('req'), may hold values from 0 to 255, as said below
- out_weight: bfloat16 [2048, 4096], P('req', 'head'), may hold values from -0.125 to 0.125
- out_bias: float32 [4096], P('head'), may hold values from -3 to 3
Outputs:
- attended: bfloat16 [32768, 4096], P('req', 'head')
- kv_pages: bfloat16 [256, 2, 128, 2048], P('req', None, None, 'head')
The draws below stay inside these ranges and needn't reach their ends.
Inputs may be any that keep to these rules, and one draw needn't show every extreme that they name: page_table is a permutation in which page b of the stream goes to one of the pages 2 * (b // 2) to 2 * (b // 2) + 1.
All inputs are finite; a program needn't handle non-finite values.
Results may differ from the reference program's by a relative error of at most 0.0046.
Values may be sent and summed in bfloat16 or wider, within the bound.
No kernel may reach another device: no remote copies, remote signals or barrier semaphores. Data moves between devices by JAX's collectives and lax.ppermute only.
A program may use at most 64 MiB of HBM per device.

```python
import math
import jax
import jax.numpy as jnp
import numpy as np
from jax import lax

HEADS = 16
DH = 128
D = 4096
ROT = 32
PAGE = 128
BLK_DEV = 2
LONG_BLK = 8
REACH = 4
TOK_DEV = 256
NBLK = 256
TOKENS = 32768
REQS = 64
N_REQ = 128


def joint_projections(key):
    shape = (TOKENS, HEADS, DH)
    query_part = jnp.clip(jax.random.normal(jax.random.fold_in(key, 11), shape, jnp.float32), -6.0, 6.0)
    key_part = jnp.clip(jax.random.normal(jax.random.fold_in(key, 12), shape, jnp.float32), -6.0, 6.0)
    return (query_part.reshape(TOKENS, HEADS * DH), key_part.reshape(TOKENS, HEADS * DH))


def draw_query_proj(key, part):
    return joint_projections(key)[0].astype(jnp.bfloat16)


def draw_key_proj(key, part):
    return joint_projections(key)[1].astype(jnp.bfloat16)


def draw_page_table(key, part):
    groups = NBLK // BLK_DEV
    group_keys = jax.random.split(jax.random.fold_in(key, 21), groups)
    orders = jax.vmap(lambda group_key: jax.random.permutation(group_key, BLK_DEV))(group_keys)
    firsts = (jnp.arange(groups, dtype=jnp.int32) * BLK_DEV)[:, None]
    return (firsts + orders.astype(jnp.int32)).reshape(NBLK).astype(jnp.int32)


def steps_of(key, shape, cuts, smallest, largest):
    gain, own = 1.0, jax.random.fold_in(key, 6)
    for axis_at, shards_of in cuts:
        steps = jnp.exp(jax.random.uniform(jax.random.fold_in(own, axis_at), (shards_of,), jnp.float32, smallest / len(cuts), largest / len(cuts)))
        gain = gain * jnp.repeat(steps, shape[axis_at] // shards_of).reshape([-1 if axis == axis_at else 1 for axis in range(len(shape))])
    return gain


def profile(amount, total, bound, slope):
    loads = [(1 << 20) // math.isqrt(grade ** slope) + 1 for grade in range(2, amount + 1)]
    rest, counts = total - bound - (amount - 1), [1] * (amount - 1)
    while rest > 0:
        free = [i for i in range(amount - 1) if counts[i] < bound]
        pool, left = sum([loads[i] for i in free]), rest
        for i in free:
            addition = min(bound - counts[i], max(1, left * loads[i] // pool), rest)
            counts[i] = counts[i] + addition
            rest = rest - addition
    return np.array([bound] + counts)


def ragged_sizes(rng, amount, total, reach, lean):
    if amount == 2:
        one = jax.random.randint(rng, (), max(1, total - reach), min(reach, total - 1) + 1)
        return jnp.stack([one, total - one])
    sizes = jnp.asarray(profile(amount, total, reach, lean), jnp.int32)
    couples = (amount - 1) // 2
    giver, receiver = sizes[1:1 + 2 * couples:2], sizes[2:2 + 2 * couples:2]
    margin = jnp.minimum(giver - 1, reach - receiver)
    passed = jax.random.randint(jax.random.fold_in(rng, 1), (couples,), 0, 1 << 20) % (margin + 1)
    sizes = sizes.at[1:1 + 2 * couples:2].set(giver - passed).at[2:2 + 2 * couples:2].set(receiver + passed)
    return sizes[jax.random.permutation(jax.random.fold_in(rng, 2), amount)]


def scatter_about(own_key, shape, scale, bound, cuts=(), kind=jnp.bfloat16):
    result = jax.random.normal(own_key, shape, jnp.float32) * scale
    if len(cuts) > 0:
        result = steps_of(own_key, shape, cuts, -0.22, 0.18) * result
    return jnp.clip(result, min=-bound, max=bound).astype(kind)


def setup_inputs(seed: int = 0) -> dict:
    streams_of = jax.random.split(jax.random.key(seed), 8)
    return {
        "query_proj": draw_query_proj(jax.random.fold_in(streams_of[7], 71), 0),
        "key_proj": draw_key_proj(jax.random.fold_in(streams_of[7], 71), 0),
        "value_proj": scatter_about(streams_of[2], (TOKENS, HEADS * DH), 1.0, 6.0, ((0, 128), (1, 4))),
        "lengths": ragged_sizes(streams_of[3], REQS, NBLK, LONG_BLK, 2).astype(jnp.int32),
        "page_table": draw_page_table(jax.random.fold_in(streams_of[7], 71), 0),
        "out_weight": scatter_about(streams_of[5], (HEADS * DH, D), (HEADS * DH) ** -0.5, 0.125, ((0, 128), (1, 4))),
        "out_bias": scatter_about(streams_of[6], (D,), 0.5, 3.0, ((0, 4),), jnp.float32),
    }


rope_base = 10000.0

def request_info(lengths, token_index):
    request_ends = jnp.cumsum(lengths).astype(jnp.int32) * PAGE
    request_starts = request_ends - lengths * PAGE
    inside = request_starts[None, :] <= token_index[:, None]
    request_id = lax.optimization_barrier(jnp.sum(inside.astype(jnp.int32), axis=1)) - 1
    opening = lax.optimization_barrier(jnp.max(jnp.where(inside, request_starts[None, :], 0), axis=1))
    return (request_id.astype(jnp.int32), (token_index - opening).astype(jnp.int32))

def rotate_heads(projected, position):
    values_f32 = projected.astype(jnp.float32)
    half_rot = ROT // 2
    frequency = jnp.exp(jnp.arange(half_rot, dtype=jnp.float32) * (-2.0 * math.log(rope_base) / ROT))
    angles = position.astype(jnp.float32)[:, None] * frequency[None, :]
    cosine = jnp.cos(angles)[:, None, :]
    sine = jnp.sin(angles)[:, None, :]
    front_half = values_f32[..., :half_rot]
    back_half = values_f32[..., half_rot:ROT]
    turned = jnp.concatenate([front_half * cosine - back_half * sine, back_half * cosine + front_half * sine, values_f32[..., ROT:]], axis=-1)
    return turned.astype(jnp.bfloat16)

def attend_block(query_rot, key_rot, value_rows, query_id, query_token, key_id, key_token):
    scores = jnp.einsum('qhd,khd->hqk', query_rot.astype(jnp.float32), key_rot.astype(jnp.float32)) * (1.0 / math.sqrt(DH))
    allowed = (query_id[:, None] == key_id[None, :]) & (key_token[None, :] <= query_token[:, None])
    scores = jnp.where(allowed[None], scores, -jnp.inf)
    row_max = lax.optimization_barrier(jnp.max(scores, axis=-1, keepdims=True))
    raised = jnp.exp(scores - row_max)
    probs = (raised / lax.optimization_barrier(jnp.sum(raised, axis=-1, keepdims=True))).astype(jnp.bfloat16)
    mixed = jnp.einsum('hqk,khd->qhd', probs.astype(jnp.float32), value_rows.astype(jnp.float32))
    return mixed.astype(jnp.bfloat16)

def reference(query_proj, key_proj, value_proj, lengths, page_table, out_weight, out_bias):
    token_index = jnp.arange(TOKENS, dtype=jnp.int32)
    request_id, position = request_info(lengths, token_index)
    query_rot = rotate_heads(query_proj.reshape(TOKENS, HEADS, DH), position)
    key_rot = rotate_heads(key_proj.reshape(TOKENS, HEADS, DH), position)
    value_rows = value_proj.reshape(TOKENS, HEADS, DH)
    key_span = REACH * TOK_DEV
    key_padded = jnp.concatenate([jnp.zeros((key_span, HEADS, DH), jnp.bfloat16), key_rot], axis=0)
    value_padded = jnp.concatenate([jnp.zeros((key_span, HEADS, DH), jnp.bfloat16), value_rows], axis=0)
    id_padded = jnp.concatenate([jnp.full((key_span,), -1, jnp.int32), request_id], axis=0)

    def one_block(block_index):
        row_start = (block_index * TOK_DEV).astype(jnp.int32)
        query_block = lax.dynamic_slice_in_dim(query_rot, row_start, TOK_DEV, 0)
        query_id = lax.dynamic_slice_in_dim(request_id, row_start, TOK_DEV, 0)
        key_block = lax.dynamic_slice_in_dim(key_padded, row_start, key_span + TOK_DEV, 0)
        value_block = lax.dynamic_slice_in_dim(value_padded, row_start, key_span + TOK_DEV, 0)
        key_id = lax.dynamic_slice_in_dim(id_padded, row_start, key_span + TOK_DEV, 0)
        query_token = row_start + jnp.arange(TOK_DEV, dtype=jnp.int32)
        key_token = row_start - key_span + jnp.arange(key_span + TOK_DEV, dtype=jnp.int32)
        return attend_block(query_block, key_block, value_block, query_id, query_token, key_id, key_token)
    mixed = lax.map(one_block, jnp.arange(N_REQ, dtype=jnp.int32))
    heads_out = mixed.reshape(TOKENS, HEADS * DH)
    attended = (jnp.dot(heads_out, out_weight, preferred_element_type=jnp.float32) + out_bias).astype(jnp.bfloat16)
    stacked = jnp.stack([key_rot.reshape(NBLK, PAGE, HEADS * DH), value_proj.reshape(NBLK, PAGE, HEADS * DH)], axis=1)
    kv_pages = jnp.zeros_like(stacked).at[page_table].set(stacked)
    return (attended, kv_pages)
```

```python
import math

import jax
import jax.numpy as jnp
from jax import lax
from jax.sharding import Mesh, PartitionSpec as P

DH = 128
ROT = 32
PAGE = 128
BLK_DEV = 2
REACH = 4
TOK_DEV = 256


rope_base = 10000.0


REQ = ("z", "x", "core")


def passed_along(array, axis, by):
    count = lax.axis_size(axis)
    pairs = [(i, i + by) for i in range(count) if 0 <= i + by < count]
    return lax.ppermute(array, axis, pairs)


def request_info(lengths, token_index):
    request_ends = jnp.cumsum(lengths) * PAGE
    request_starts = request_ends - lengths * PAGE
    inside = request_starts[None, :] <= token_index[:, None]
    request_id = jnp.sum(inside.astype(jnp.int32), axis=1) - 1
    opening = jnp.max(jnp.where(inside, request_starts[None, :], 0), axis=1)
    return (request_id, token_index - opening)


def rotate_heads(projected, position):
    values_f32 = projected.astype(jnp.float32)
    half_rot = ROT // 2
    frequency = jnp.exp(
        jnp.arange(half_rot, dtype=jnp.float32) * (-2.0 * math.log(rope_base) / ROT)
    )
    angles = position.astype(jnp.float32)[:, None] * frequency[None, :]
    cosine = jnp.cos(angles)[:, None, :]
    sine = jnp.sin(angles)[:, None, :]
    front_half = values_f32[..., :half_rot]
    back_half = values_f32[..., half_rot:ROT]
    turned = jnp.concatenate(
        [
            front_half * cosine - back_half * sine,
            back_half * cosine + front_half * sine,
            values_f32[..., ROT:],
        ],
        axis=-1,
    )
    return turned.astype(jnp.bfloat16)


def attend_block(query_rot, key_rot, value_rows, query_id, query_token, key_id, key_token):
    scores = jnp.einsum("qhd,khd->hqk", query_rot, key_rot, preferred_element_type=jnp.float32) * (
        1.0 / math.sqrt(DH)
    )
    allowed = (query_id[:, None] == key_id[None, :]) & (key_token[None, :] <= query_token[:, None])
    scores = jnp.where(allowed[None], scores, -jnp.inf)
    row_max = jnp.max(scores, axis=-1, keepdims=True)
    raised = jnp.exp(scores - row_max)
    probs = (raised / jnp.sum(raised, axis=-1, keepdims=True)).astype(jnp.bfloat16)
    mixed = jnp.einsum("hqk,khd->qhd", probs, value_rows, preferred_element_type=jnp.float32)
    return mixed.astype(jnp.bfloat16)


def local(query_proj, key_proj, value_proj, lengths, page_table, out_weight, out_bias):
    local_heads = query_proj.shape[1] // DH
    device_rank = lax.axis_index(REQ)
    first_token = device_rank * TOK_DEV
    own_tokens = first_token + jnp.arange(TOK_DEV, dtype=jnp.int32)
    request_id, position = request_info(lengths, own_tokens)
    query_rot = rotate_heads(query_proj.reshape(TOK_DEV, local_heads, DH), position)
    key_flat = rotate_heads(key_proj.reshape(TOK_DEV, local_heads, DH), position).reshape(
        TOK_DEV, local_heads * DH
    )
    key_list = [key_flat]
    value_list = [value_proj]
    for distance in range(1, REACH + 1):
        far_key, far_value = passed_along((key_flat, value_proj), REQ, distance)
        key_list.append(far_key)
        value_list.append(far_value)
    key_stack = jnp.stack(key_list[::-1], axis=0)
    value_stack = jnp.stack(value_list[::-1], axis=0)
    key_rows = (REACH + 1) * TOK_DEV
    key_all = key_stack.reshape(key_rows, local_heads, DH)
    value_all = value_stack.reshape(key_rows, local_heads, DH)
    key_tokens = first_token - REACH * TOK_DEV + jnp.arange(key_rows, dtype=jnp.int32)
    key_id, key_position = request_info(lengths, key_tokens)
    mixed = attend_block(query_rot, key_all, value_all, request_id, own_tokens, key_id, key_tokens)
    heads_out = mixed.reshape(TOK_DEV, local_heads * DH)
    weight_rows = lax.all_gather(out_weight, "core", axis=0, tiled=True)
    weight_rows = lax.all_gather(weight_rows, "x", axis=0, tiled=True)
    weight_rows = lax.all_gather(weight_rows, "z", axis=0, tiled=True)
    heads_all = lax.all_gather(heads_out, "head", axis=1, tiled=True)
    summed = jnp.dot(heads_all, weight_rows, preferred_element_type=jnp.float32)
    attended = (summed + out_bias).astype(jnp.bfloat16)
    local_page = page_table - device_rank * BLK_DEV
    picker = (local_page[:, None] == jnp.arange(BLK_DEV, dtype=jnp.int32)[None, :]).astype(
        jnp.bfloat16
    )
    page_blocks = jnp.stack(
        [
            key_flat.reshape(BLK_DEV, PAGE, local_heads * DH),
            value_proj.reshape(BLK_DEV, PAGE, local_heads * DH),
        ],
        axis=1,
    )
    kv_pages = jnp.einsum(
        "bp,bctd->pctd", picker, page_blocks, preferred_element_type=jnp.float32
    ).astype(jnp.bfloat16)
    return (attended, kv_pages)


def solution(mesh):
    devices = mesh.devices
    cores = len({d.core_on_chip for d in devices.flat})
    columns = len({d.coords[0] for d in devices.flat})
    req_size, head_size = devices.shape
    split = Mesh(
        devices.reshape(req_size // (columns * cores), columns, cores, head_size),
        ("z", "x", "core", "head"),
    )
    placed = (
        P(REQ, "head"),
        P(REQ, "head"),
        P(REQ, "head"),
        P(),
        P(REQ),
        P(REQ, "head"),
        P("head"),
    )
    return jax.shard_map(
        local,
        mesh=split,
        in_specs=placed,
        out_specs=(P(REQ, "head"), P(REQ, None, None, "head")),
        check_vma=False,
    )
```

```python
import math

import jax
import jax.numpy as jnp
from jax import lax
from jax.sharding import Mesh, PartitionSpec as P


DH = 128
ROT = 32
PAGE = 128
BLK_DEV = 2
REACH = 4
TOK_DEV = 256


rope_base = 10000.0


REQ = ("z", "x", "core")


def passed_along(array, axis, by):
    count = lax.axis_size(axis)
    pairs = [(i, i + by) for i in range(count) if 0 <= i + by < count]
    return lax.ppermute(array, axis, pairs)


def request_info(lengths, token_index):
    request_ends = jnp.cumsum(lengths) * PAGE
    request_starts = request_ends - lengths * PAGE
    inside = request_starts[None, :] <= token_index[:, None]
    request_id = jnp.sum(inside.astype(jnp.int32), axis=1) - 1
    opening = jnp.max(jnp.where(inside, request_starts[None, :], 0), axis=1)
    return (request_id, token_index - opening)


def rotate_heads(projected, position):
    values_f32 = projected.astype(jnp.float32)
    half_rot = ROT // 2
    frequency = jnp.exp(
        jnp.arange(half_rot, dtype=jnp.float32) * (-2.0 * math.log(rope_base) / ROT)
    )
    angles = position.astype(jnp.float32)[:, None] * frequency[None, :]
    cosine = jnp.cos(angles)[:, None, :]
    sine = jnp.sin(angles)[:, None, :]
    front_half = values_f32[..., :half_rot]
    back_half = values_f32[..., half_rot:ROT]
    turned = jnp.concatenate(
        [
            front_half * cosine - back_half * sine,
            back_half * cosine + front_half * sine,
            values_f32[..., ROT:],
        ],
        axis=-1,
    )
    return turned.astype(jnp.bfloat16)


def attend_block(query_rot, key_rot, value_rows, query_id, query_token, key_id, key_token):
    scores = jnp.einsum("qhd,khd->hqk", query_rot, key_rot, preferred_element_type=jnp.float32) * (
        1.0 / math.sqrt(DH)
    )
    allowed = (query_id[:, None] == key_id[None, :]) & (key_token[None, :] <= query_token[:, None])
    scores = jnp.where(allowed[None], scores, -jnp.inf)
    row_max = jnp.max(scores, axis=-1, keepdims=True)
    raised = jnp.exp(scores - row_max)
    probs = (raised / jnp.sum(raised, axis=-1, keepdims=True)).astype(jnp.bfloat16)
    mixed = jnp.einsum("hqk,khd->qhd", probs, value_rows, preferred_element_type=jnp.float32)
    return mixed.astype(jnp.bfloat16)


def local_body(query_proj, key_proj, value_proj, lengths, page_table, out_weight, out_bias):
    local_heads = query_proj.shape[1] // DH
    device_rank = lax.axis_index(REQ)
    core_rank = lax.axis_index("core")
    half = out_weight.shape[1] // 2
    weight_pair = lax.all_gather(out_weight, "core", axis=0, tiled=True)
    weight_rows = lax.dynamic_slice_in_dim(weight_pair, core_rank * half, half, 1)
    weight_rows = lax.all_gather(weight_rows, "x", axis=0, tiled=True)
    weight_rows, query_proj, key_proj = lax.optimization_barrier(
        (weight_rows, query_proj, key_proj)
    )
    weight_rows = lax.all_gather(weight_rows, "z", axis=0, tiled=True)
    first_token = device_rank * TOK_DEV
    own_tokens = first_token + jnp.arange(TOK_DEV, dtype=jnp.int32)
    request_id, position = request_info(lengths, own_tokens)
    query_rot = rotate_heads(query_proj.reshape(TOK_DEV, local_heads, DH), position)
    key_flat = rotate_heads(key_proj.reshape(TOK_DEV, local_heads, DH), position).reshape(
        TOK_DEV, local_heads * DH
    )
    halo = jnp.stack([key_flat, value_proj], axis=0)
    halo_list = [halo]
    for distance in range(1, REACH + 1):
        halo_list.append(passed_along(halo, REQ, distance))
    halo_stack = jnp.stack(halo_list[::-1], axis=1)
    key_stack = halo_stack[0]
    value_stack = halo_stack[1]
    key_rows = (REACH + 1) * TOK_DEV
    key_all = key_stack.reshape(key_rows, local_heads, DH)
    value_all = value_stack.reshape(key_rows, local_heads, DH)
    key_tokens = first_token - REACH * TOK_DEV + jnp.arange(key_rows, dtype=jnp.int32)
    key_id, _ = request_info(lengths, key_tokens)
    mixed = attend_block(query_rot, key_all, value_all, request_id, own_tokens, key_id, key_tokens)
    heads_out = mixed.reshape(TOK_DEV, local_heads * DH)
    heads_all = lax.all_gather(heads_out, "head", axis=1, tiled=True)
    heads_pair = lax.all_gather(heads_all, "core", axis=0, tiled=True)
    summed = jnp.dot(heads_pair, weight_rows, preferred_element_type=jnp.float32)
    bias_half = lax.dynamic_slice_in_dim(out_bias, core_rank * half, half, 0)
    pair_out = (summed + bias_half).astype(jnp.bfloat16)
    attended = lax.all_to_all(
        pair_out.reshape(2, TOK_DEV, half), "core", 0, 2, tiled=True
    ).reshape(TOK_DEV, 2 * half)
    local_page = page_table - device_rank * BLK_DEV
    picker = (local_page[:, None] == jnp.arange(BLK_DEV, dtype=jnp.int32)[None, :]).astype(
        jnp.bfloat16
    )
    page_blocks = jnp.stack(
        [
            key_flat.reshape(BLK_DEV, PAGE, local_heads * DH),
            value_proj.reshape(BLK_DEV, PAGE, local_heads * DH),
        ],
        axis=1,
    )
    kv_pages = jnp.einsum(
        "bp,bctd->pctd", picker, page_blocks, preferred_element_type=jnp.float32
    ).astype(jnp.bfloat16)
    return (attended, kv_pages)


def solution(mesh):
    devices = mesh.devices
    cores = len({d.core_on_chip for d in devices.flat})
    columns = len({d.coords[0] for d in devices.flat})
    req_size, head_size = devices.shape
    split = Mesh(
        devices.reshape(req_size // (columns * cores), columns, cores, head_size),
        ("z", "x", "core", "head"),
    )
    placed = (
        P(REQ, "head"),
        P(REQ, "head"),
        P(REQ, "head"),
        P(),
        P(REQ),
        P(REQ, "head"),
        P("head"),
    )
    return jax.shard_map(
        local_body,
        mesh=split,
        in_specs=placed,
        out_specs=(P(REQ, "head"), P(REQ, None, None, "head")),
        check_vma=False,
    )
```

```python
import math

import jax
import jax.numpy as jnp
from jax import lax
from jax.sharding import Mesh, PartitionSpec as P


DH = 128
ROT = 32
PAGE = 128
BLK_DEV = 2
REACH = 4
TOK_DEV = 256


rope_base = 10000.0


REQ = ("z", "x", "core")


def passed_along(array, axis, by):
    count = lax.axis_size(axis)
    pairs = [(i, i + by) for i in range(count) if 0 <= i + by < count]
    return lax.ppermute(array, axis, pairs)


def swapped(array, axis):
    return lax.ppermute(array, axis, [(0, 1), (1, 0)])


def ring_gather(piece, axis):
    count = lax.axis_size(axis)
    forward = [(i, (i + 1) % count) for i in range(count)]
    backward = [(i, (i - 1) % count) for i in range(count)]
    ahead = [piece]
    behind = []
    sent_ahead = piece
    sent_behind = piece
    for step in range(1, count // 2 + 1):
        sent_ahead = lax.ppermute(sent_ahead, axis, forward)
        behind.append(sent_ahead)
        if step < count - count // 2:
            sent_behind = lax.ppermute(sent_behind, axis, backward)
            ahead.append(sent_behind)
    relative = jnp.stack(ahead + behind[::-1], axis=0)
    rank = lax.axis_index(axis)
    placed = jnp.roll(relative, rank, axis=0)
    return placed.reshape((count * piece.shape[0],) + piece.shape[1:])


def request_info(lengths, token_index):
    request_ends = jnp.cumsum(lengths) * PAGE
    request_starts = request_ends - lengths * PAGE
    inside = request_starts[None, :] <= token_index[:, None]
    request_id = jnp.sum(inside.astype(jnp.int32), axis=1) - 1
    opening = jnp.max(jnp.where(inside, request_starts[None, :], 0), axis=1)
    return (request_id, token_index - opening)


def rotate_heads(projected, position):
    values_f32 = projected.astype(jnp.float32)
    half_rot = ROT // 2
    frequency = jnp.exp(
        jnp.arange(half_rot, dtype=jnp.float32) * (-2.0 * math.log(rope_base) / ROT)
    )
    angles = position.astype(jnp.float32)[:, None] * frequency[None, :]
    cosine = jnp.cos(angles)[:, None, :]
    sine = jnp.sin(angles)[:, None, :]
    front_half = values_f32[..., :half_rot]
    back_half = values_f32[..., half_rot:ROT]
    turned = jnp.concatenate(
        [
            front_half * cosine - back_half * sine,
            back_half * cosine + front_half * sine,
            values_f32[..., ROT:],
        ],
        axis=-1,
    )
    return turned.astype(jnp.bfloat16)


def attend_block(query_rot, key_rot, value_rows, query_id, query_token, key_id, key_token):
    scores = jnp.einsum("qhd,khd->hqk", query_rot, key_rot, preferred_element_type=jnp.float32) * (
        1.0 / math.sqrt(DH)
    )
    allowed = (query_id[:, None] == key_id[None, :]) & (key_token[None, :] <= query_token[:, None])
    scores = jnp.where(allowed[None], scores, -jnp.inf)
    row_max = jnp.max(scores, axis=-1, keepdims=True)
    raised = jnp.exp(scores - row_max)
    probs = (raised / jnp.sum(raised, axis=-1, keepdims=True)).astype(jnp.bfloat16)
    mixed = jnp.einsum("hqk,khd->qhd", probs, value_rows, preferred_element_type=jnp.float32)
    return mixed.astype(jnp.bfloat16)


def local_body(query_proj, key_proj, value_proj, lengths, page_table, out_weight, out_bias):
    local_heads = query_proj.shape[1] // DH
    device_rank = lax.axis_index(REQ)
    core_rank = lax.axis_index("core")
    half = out_weight.shape[1] // 2
    weight_pair = lax.all_gather(out_weight, "core", axis=0, tiled=True)
    weight_rows = lax.dynamic_slice_in_dim(weight_pair, core_rank * half, half, 1)
    weight_rows = ring_gather(weight_rows, "x")
    weight_rows = ring_gather(weight_rows, "z")
    weight_other = swapped(weight_rows, "core")
    first_token = device_rank * TOK_DEV
    own_tokens = first_token + jnp.arange(TOK_DEV, dtype=jnp.int32)
    request_id, position = request_info(lengths, own_tokens)
    query_rot = rotate_heads(query_proj.reshape(TOK_DEV, local_heads, DH), position)
    key_flat = rotate_heads(key_proj.reshape(TOK_DEV, local_heads, DH), position).reshape(
        TOK_DEV, local_heads * DH
    )
    halo = jnp.stack([key_flat, value_proj], axis=0)
    halo_list = [halo]
    for distance in range(1, REACH + 1):
        halo_list.append(passed_along(halo, REQ, distance))
    halo_stack = jnp.stack(halo_list[::-1], axis=1)
    key_stack = halo_stack[0]
    value_stack = halo_stack[1]
    key_rows = (REACH + 1) * TOK_DEV
    key_all = key_stack.reshape(key_rows, local_heads, DH)
    value_all = value_stack.reshape(key_rows, local_heads, DH)
    key_tokens = first_token - REACH * TOK_DEV + jnp.arange(key_rows, dtype=jnp.int32)
    key_id, _ = request_info(lengths, key_tokens)
    weight_rows, weight_other, query_rot = lax.optimization_barrier(
        (weight_rows, weight_other, query_rot)
    )
    mixed = attend_block(query_rot, key_all, value_all, request_id, own_tokens, key_id, key_tokens)
    heads_out = mixed.reshape(TOK_DEV, local_heads * DH)
    heads_all = ring_gather(heads_out.T, "head").T
    other_rank = 1 - core_rank
    bias_own = lax.dynamic_slice_in_dim(out_bias, core_rank * half, half, 0)
    bias_other = lax.dynamic_slice_in_dim(out_bias, other_rank * half, half, 0)
    own_cols = jnp.dot(heads_all, weight_rows, preferred_element_type=jnp.float32) + bias_own
    other_cols = jnp.dot(heads_all, weight_other, preferred_element_type=jnp.float32) + bias_other
    own_cols = own_cols.astype(jnp.bfloat16)
    other_cols = other_cols.astype(jnp.bfloat16)
    attended = jnp.where(
        core_rank == 0,
        jnp.concatenate([own_cols, other_cols], axis=1),
        jnp.concatenate([other_cols, own_cols], axis=1),
    )
    local_page = page_table - device_rank * BLK_DEV
    picker = (local_page[:, None] == jnp.arange(BLK_DEV, dtype=jnp.int32)[None, :]).astype(
        jnp.bfloat16
    )
    page_blocks = jnp.stack(
        [
            key_flat.reshape(BLK_DEV, PAGE, local_heads * DH),
            value_proj.reshape(BLK_DEV, PAGE, local_heads * DH),
        ],
        axis=1,
    )
    kv_pages = jnp.einsum(
        "bp,bctd->pctd", picker, page_blocks, preferred_element_type=jnp.float32
    ).astype(jnp.bfloat16)
    return (attended, kv_pages)


def solution(mesh):
    devices = mesh.devices
    cores = len({d.core_on_chip for d in devices.flat})
    columns = len({d.coords[0] for d in devices.flat})
    req_size, head_size = devices.shape
    split = Mesh(
        devices.reshape(req_size // (columns * cores), columns, cores, head_size),
        ("z", "x", "core", "head"),
    )
    placed = (
        P(REQ, "head"),
        P(REQ, "head"),
        P(REQ, "head"),
        P(),
        P(REQ),
        P(REQ, "head"),
        P("head"),
    )
    return jax.shard_map(
        local_body,
        mesh=split,
        in_specs=placed,
        out_specs=(P(REQ, "head"), P(REQ, None, None, "head")),
        check_vma=False,
    )
```

```python
import math

import jax
import jax.numpy as jnp
from jax import lax
from jax.sharding import Mesh, PartitionSpec as P


DH = 128
ROT = 32
PAGE = 128
BLK_DEV = 2
REACH = 4
TOK_DEV = 256


rope_base = 10000.0


REQ = ("z", "x", "core")


def passed_along(array, axis, by):
    count = lax.axis_size(axis)
    pairs = [(i, i + by) for i in range(count) if 0 <= i + by < count]
    return lax.ppermute(array, axis, pairs)


def request_info(lengths, token_index):
    request_ends = jnp.cumsum(lengths) * PAGE
    request_starts = request_ends - lengths * PAGE
    inside = request_starts[None, :] <= token_index[:, None]
    request_id = jnp.sum(inside.astype(jnp.int32), axis=1) - 1
    opening = jnp.max(jnp.where(inside, request_starts[None, :], 0), axis=1)
    return (request_id, token_index - opening)


def rotate_heads(projected, position):
    values_f32 = projected.astype(jnp.float32)
    half_rot = ROT // 2
    frequency = jnp.exp(
        jnp.arange(half_rot, dtype=jnp.float32) * (-2.0 * math.log(rope_base) / ROT)
    )
    angles = position.astype(jnp.float32)[:, None] * frequency[None, :]
    cosine = jnp.cos(angles)[:, None, :]
    sine = jnp.sin(angles)[:, None, :]
    front_half = values_f32[..., :half_rot]
    back_half = values_f32[..., half_rot:ROT]
    turned = jnp.concatenate(
        [
            front_half * cosine - back_half * sine,
            back_half * cosine + front_half * sine,
            values_f32[..., ROT:],
        ],
        axis=-1,
    )
    return turned.astype(jnp.bfloat16)


def attend_block(query_rot, key_rot, value_rows, query_id, query_token, key_id, key_token):
    scores = jnp.einsum("qhd,khd->hqk", query_rot, key_rot, preferred_element_type=jnp.float32) * (
        1.0 / math.sqrt(DH)
    )
    allowed = (query_id[:, None] == key_id[None, :]) & (key_token[None, :] <= query_token[:, None])
    scores = jnp.where(allowed[None], scores, -jnp.inf)
    row_max = jnp.max(scores, axis=-1, keepdims=True)
    raised = jnp.exp(scores - row_max)
    probs = (raised / jnp.sum(raised, axis=-1, keepdims=True)).astype(jnp.bfloat16)
    mixed = jnp.einsum("hqk,khd->qhd", probs, value_rows, preferred_element_type=jnp.float32)
    return mixed.astype(jnp.bfloat16)


def local_body(query_proj, key_proj, value_proj, lengths, page_table, out_weight, out_bias):
    local_heads = query_proj.shape[1] // DH
    device_rank = lax.axis_index(REQ)
    core_rank = lax.axis_index("core")
    half = out_weight.shape[1] // 2
    weight_pair = lax.all_gather(out_weight, "core", axis=0, tiled=True)
    weight_rows = lax.dynamic_slice_in_dim(weight_pair, core_rank * half, half, 1)
    weight_rows = lax.all_gather(weight_rows, "x", axis=0, tiled=True)
    weight_rows, query_proj, key_proj = lax.optimization_barrier(
        (weight_rows, query_proj, key_proj)
    )
    weight_rows = lax.all_gather(weight_rows, "z", axis=0, tiled=True)
    weight_other = lax.ppermute(weight_rows, "core", [(0, 1), (1, 0)])
    first_token = device_rank * TOK_DEV
    own_tokens = first_token + jnp.arange(TOK_DEV, dtype=jnp.int32)
    request_id, position = request_info(lengths, own_tokens)
    query_rot = rotate_heads(query_proj.reshape(TOK_DEV, local_heads, DH), position)
    key_flat = rotate_heads(key_proj.reshape(TOK_DEV, local_heads, DH), position).reshape(
        TOK_DEV, local_heads * DH
    )
    halo = jnp.stack([key_flat, value_proj], axis=0)
    halo_list = [halo]
    for distance in range(1, REACH + 1):
        halo_list.append(passed_along(halo, REQ, distance))
    halo_stack = jnp.stack(halo_list[::-1], axis=1)
    key_stack = halo_stack[0]
    value_stack = halo_stack[1]
    key_rows = (REACH + 1) * TOK_DEV
    key_all = key_stack.reshape(key_rows, local_heads, DH)
    value_all = value_stack.reshape(key_rows, local_heads, DH)
    key_tokens = first_token - REACH * TOK_DEV + jnp.arange(key_rows, dtype=jnp.int32)
    key_id, _ = request_info(lengths, key_tokens)
    mixed = attend_block(query_rot, key_all, value_all, request_id, own_tokens, key_id, key_tokens)
    heads_out = mixed.reshape(TOK_DEV, local_heads * DH)
    heads_all = lax.all_gather(heads_out, "head", axis=1, tiled=True)
    other_rank = 1 - core_rank
    bias_own = lax.dynamic_slice_in_dim(out_bias, core_rank * half, half, 0)
    bias_other = lax.dynamic_slice_in_dim(out_bias, other_rank * half, half, 0)
    own_cols = jnp.dot(heads_all, weight_rows, preferred_element_type=jnp.float32) + bias_own
    other_cols = jnp.dot(heads_all, weight_other, preferred_element_type=jnp.float32) + bias_other
    own_cols = own_cols.astype(jnp.bfloat16)
    other_cols = other_cols.astype(jnp.bfloat16)
    attended = jnp.where(
        core_rank == 0,
        jnp.concatenate([own_cols, other_cols], axis=1),
        jnp.concatenate([other_cols, own_cols], axis=1),
    )
    local_page = page_table - device_rank * BLK_DEV
    picker = (local_page[:, None] == jnp.arange(BLK_DEV, dtype=jnp.int32)[None, :]).astype(
        jnp.bfloat16
    )
    page_blocks = jnp.stack(
        [
            key_flat.reshape(BLK_DEV, PAGE, local_heads * DH),
            value_proj.reshape(BLK_DEV, PAGE, local_heads * DH),
        ],
        axis=1,
    )
    kv_pages = jnp.einsum(
        "bp,bctd->pctd", picker, page_blocks, preferred_element_type=jnp.float32
    ).astype(jnp.bfloat16)
    return (attended, kv_pages)


def solution(mesh):
    devices = mesh.devices
    cores = len({d.core_on_chip for d in devices.flat})
    columns = len({d.coords[0] for d in devices.flat})
    req_size, head_size = devices.shape
    split = Mesh(
        devices.reshape(req_size // (columns * cores), columns, cores, head_size),
        ("z", "x", "core", "head"),
    )
    placed = (
        P(REQ, "head"),
        P(REQ, "head"),
        P(REQ, "head"),
        P(),
        P(REQ),
        P(REQ, "head"),
        P("head"),
    )
    return jax.shard_map(
        local_body,
        mesh=split,
        in_specs=placed,
        out_specs=(P(REQ, "head"), P(REQ, None, None, "head")),
        check_vma=False,
    )
```

```python
import math

import jax
import jax.numpy as jnp
from jax import lax
from jax.sharding import Mesh, PartitionSpec as P


DH = 128
ROT = 32
PAGE = 128
BLK_DEV = 2
REACH = 4
TOK_DEV = 256


rope_base = 10000.0


REQ = ("z", "x", "core")


def passed_along(array, axis, by):
    count = lax.axis_size(axis)
    pairs = [(i, i + by) for i in range(count) if 0 <= i + by < count]
    return lax.ppermute(array, axis, pairs)


def request_info(lengths, token_index):
    request_ends = jnp.cumsum(lengths) * PAGE
    request_starts = request_ends - lengths * PAGE
    inside = request_starts[None, :] <= token_index[:, None]
    request_id = jnp.sum(inside.astype(jnp.int32), axis=1) - 1
    opening = jnp.max(jnp.where(inside, request_starts[None, :], 0), axis=1)
    return (request_id, token_index - opening)


def rotate_heads(projected, position):
    values_f32 = projected.astype(jnp.float32)
    half_rot = ROT // 2
    frequency = jnp.exp(
        jnp.arange(half_rot, dtype=jnp.float32) * (-2.0 * math.log(rope_base) / ROT)
    )
    angles = position.astype(jnp.float32)[:, None] * frequency[None, :]
    cosine = jnp.cos(angles)[:, None, :]
    sine = jnp.sin(angles)[:, None, :]
    front_half = values_f32[..., :half_rot]
    back_half = values_f32[..., half_rot:ROT]
    turned = jnp.concatenate(
        [
            front_half * cosine - back_half * sine,
            back_half * cosine + front_half * sine,
            values_f32[..., ROT:],
        ],
        axis=-1,
    )
    return turned.astype(jnp.bfloat16)


def attend_block(query_rot, key_rot, value_rows, query_id, query_token, key_id, key_token):
    scores = jnp.einsum("qhd,khd->hqk", query_rot, key_rot, preferred_element_type=jnp.float32) * (
        1.0 / math.sqrt(DH)
    )
    allowed = (query_id[:, None] == key_id[None, :]) & (key_token[None, :] <= query_token[:, None])
    scores = jnp.where(allowed[None], scores, -jnp.inf)
    row_max = jnp.max(scores, axis=-1, keepdims=True)
    raised = jnp.exp(scores - row_max)
    probs = (raised / jnp.sum(raised, axis=-1, keepdims=True)).astype(jnp.bfloat16)
    mixed = jnp.einsum("hqk,khd->qhd", probs, value_rows, preferred_element_type=jnp.float32)
    return mixed.astype(jnp.bfloat16)


def local_body(query_proj, key_proj, value_proj, lengths, page_table, out_weight, out_bias):
    local_heads = query_proj.shape[1] // DH
    device_rank = lax.axis_index(REQ)
    core_rank = lax.axis_index("core")
    half = out_weight.shape[1] // 2
    weight_pair = lax.all_gather(out_weight, "core", axis=0, tiled=True)
    weight_rows = lax.dynamic_slice_in_dim(weight_pair, core_rank * half, half, 1)
    weight_rows = lax.all_gather(weight_rows, "z", axis=0, tiled=False)
    weight_rows = lax.all_gather(weight_rows, "x", axis=1, tiled=False)
    weight_rows = weight_rows.reshape(-1, half)
    weight_other = lax.ppermute(weight_rows, "core", [(0, 1), (1, 0)])
    first_token = device_rank * TOK_DEV
    own_tokens = first_token + jnp.arange(TOK_DEV, dtype=jnp.int32)
    request_id, position = request_info(lengths, own_tokens)
    query_rot = rotate_heads(query_proj.reshape(TOK_DEV, local_heads, DH), position)
    key_flat = rotate_heads(key_proj.reshape(TOK_DEV, local_heads, DH), position).reshape(
        TOK_DEV, local_heads * DH
    )
    halo = jnp.stack([key_flat, value_proj], axis=0)
    halo_list = [halo]
    for distance in range(1, REACH + 1):
        halo_list.append(passed_along(halo, REQ, distance))
    halo_stack = jnp.stack(halo_list[::-1], axis=1)
    key_stack = halo_stack[0]
    value_stack = halo_stack[1]
    key_rows = (REACH + 1) * TOK_DEV
    key_all = key_stack.reshape(key_rows, local_heads, DH)
    value_all = value_stack.reshape(key_rows, local_heads, DH)
    key_tokens = first_token - REACH * TOK_DEV + jnp.arange(key_rows, dtype=jnp.int32)
    key_id, _ = request_info(lengths, key_tokens)
    mixed = attend_block(query_rot, key_all, value_all, request_id, own_tokens, key_id, key_tokens)
    heads_out = mixed.reshape(TOK_DEV, local_heads * DH)
    heads_all = lax.all_gather(heads_out, "head", axis=1, tiled=True)
    other_rank = 1 - core_rank
    bias_own = lax.dynamic_slice_in_dim(out_bias, core_rank * half, half, 0)
    bias_other = lax.dynamic_slice_in_dim(out_bias, other_rank * half, half, 0)
    own_cols = jnp.dot(heads_all, weight_rows, preferred_element_type=jnp.float32) + bias_own
    other_cols = jnp.dot(heads_all, weight_other, preferred_element_type=jnp.float32) + bias_other
    own_cols = own_cols.astype(jnp.bfloat16)
    other_cols = other_cols.astype(jnp.bfloat16)
    attended = jnp.where(
        core_rank == 0,
        jnp.concatenate([own_cols, other_cols], axis=1),
        jnp.concatenate([other_cols, own_cols], axis=1),
    )
    local_page = page_table - device_rank * BLK_DEV
    picker = (local_page[:, None] == jnp.arange(BLK_DEV, dtype=jnp.int32)[None, :]).astype(
        jnp.bfloat16
    )
    page_blocks = jnp.stack(
        [
            key_flat.reshape(BLK_DEV, PAGE, local_heads * DH),
            value_proj.reshape(BLK_DEV, PAGE, local_heads * DH),
        ],
        axis=1,
    )
    kv_pages = jnp.einsum(
        "bp,bctd->pctd", picker, page_blocks, preferred_element_type=jnp.float32
    ).astype(jnp.bfloat16)
    return (attended, kv_pages)


def solution(mesh):
    devices = mesh.devices
    cores = len({d.core_on_chip for d in devices.flat})
    columns = len({d.coords[0] for d in devices.flat})
    req_size, head_size = devices.shape
    split = Mesh(
        devices.reshape(req_size // (columns * cores), columns, cores, head_size),
        ("z", "x", "core", "head"),
    )
    placed = (
        P(REQ, "head"),
        P(REQ, "head"),
        P(REQ, "head"),
        P(),
        P(REQ),
        P(REQ, "head"),
        P("head"),
    )
    return jax.shard_map(
        local_body,
        mesh=split,
        in_specs=placed,
        out_specs=(P(REQ, "head"), P(REQ, None, None, "head")),
        check_vma=False,
    )
```

```python
import math

import jax
import jax.numpy as jnp
from jax import lax
from jax.sharding import Mesh, PartitionSpec as P


DH = 128
ROT = 32
PAGE = 128
BLK_DEV = 2
REACH = 4
TOK_DEV = 256


rope_base = 10000.0


REQ = ("z", "x", "core")


def passed_along(array, axis, by):
    count = lax.axis_size(axis)
    pairs = [(i, i + by) for i in range(count) if 0 <= i + by < count]
    return lax.ppermute(array, axis, pairs)


def ring_gather(piece, axis):
    count = lax.axis_size(axis)
    relative = [piece]
    for distance in range(1, count):
        pairs = [(i, (i - distance) % count) for i in range(count)]
        relative.append(lax.ppermute(piece, axis, pairs))
    return jnp.roll(jnp.stack(relative, axis=0), lax.axis_index(axis), axis=0)


def request_info(lengths, token_index):
    request_ends = jnp.cumsum(lengths) * PAGE
    request_starts = request_ends - lengths * PAGE
    inside = request_starts[None, :] <= token_index[:, None]
    request_id = jnp.sum(inside.astype(jnp.int32), axis=1) - 1
    opening = jnp.max(jnp.where(inside, request_starts[None, :], 0), axis=1)
    return (request_id, token_index - opening)


def rotate_heads(projected, position):
    values_f32 = projected.astype(jnp.float32)
    half_rot = ROT // 2
    frequency = jnp.exp(
        jnp.arange(half_rot, dtype=jnp.float32) * (-2.0 * math.log(rope_base) / ROT)
    )
    angles = position.astype(jnp.float32)[:, None] * frequency[None, :]
    cosine = jnp.cos(angles)[:, None, :]
    sine = jnp.sin(angles)[:, None, :]
    front_half = values_f32[..., :half_rot]
    back_half = values_f32[..., half_rot:ROT]
    turned = jnp.concatenate(
        [
            front_half * cosine - back_half * sine,
            back_half * cosine + front_half * sine,
            values_f32[..., ROT:],
        ],
        axis=-1,
    )
    return turned.astype(jnp.bfloat16)


def attend_block(query_rot, key_rot, value_rows, query_id, query_token, key_id, key_token):
    scores = jnp.einsum("qhd,khd->hqk", query_rot, key_rot, preferred_element_type=jnp.float32) * (
        1.0 / math.sqrt(DH)
    )
    allowed = (query_id[:, None] == key_id[None, :]) & (key_token[None, :] <= query_token[:, None])
    scores = jnp.where(allowed[None], scores, -jnp.inf)
    row_max = jnp.max(scores, axis=-1, keepdims=True)
    raised = jnp.exp(scores - row_max)
    probs = (raised / jnp.sum(raised, axis=-1, keepdims=True)).astype(jnp.bfloat16)
    mixed = jnp.einsum("hqk,khd->qhd", probs, value_rows, preferred_element_type=jnp.float32)
    return mixed.astype(jnp.bfloat16)


def local_body(query_proj, key_proj, value_proj, lengths, page_table, out_weight, out_bias):
    local_heads = query_proj.shape[1] // DH
    device_rank = lax.axis_index(REQ)
    core_rank = lax.axis_index("core")
    half = out_weight.shape[1] // 2
    weight_pair = lax.all_gather(out_weight, "core", axis=0, tiled=True)
    weight_rows = lax.dynamic_slice_in_dim(weight_pair, core_rank * half, half, 1)
    weight_rows = lax.all_gather(weight_rows, "x", axis=0, tiled=True)
    weight_rows, query_proj, key_proj = lax.optimization_barrier(
        (weight_rows, query_proj, key_proj)
    )
    weight_rows = lax.all_gather(weight_rows, "z", axis=0, tiled=True)
    weight_other = lax.ppermute(weight_rows, "core", [(0, 1), (1, 0)])
    first_token = device_rank * TOK_DEV
    own_tokens = first_token + jnp.arange(TOK_DEV, dtype=jnp.int32)
    request_id, position = request_info(lengths, own_tokens)
    query_rot = rotate_heads(query_proj.reshape(TOK_DEV, local_heads, DH), position)
    key_flat = rotate_heads(key_proj.reshape(TOK_DEV, local_heads, DH), position).reshape(
        TOK_DEV, local_heads * DH
    )
    halo = jnp.stack([key_flat, value_proj], axis=0)
    halo_list = [halo]
    for distance in range(1, REACH + 1):
        halo_list.append(passed_along(halo, REQ, distance))
    halo_stack = jnp.stack(halo_list[::-1], axis=1)
    key_stack = halo_stack[0]
    value_stack = halo_stack[1]
    key_rows = (REACH + 1) * TOK_DEV
    key_all = key_stack.reshape(key_rows, local_heads, DH)
    value_all = value_stack.reshape(key_rows, local_heads, DH)
    key_tokens = first_token - REACH * TOK_DEV + jnp.arange(key_rows, dtype=jnp.int32)
    key_id, _ = request_info(lengths, key_tokens)
    mixed = attend_block(query_rot, key_all, value_all, request_id, own_tokens, key_id, key_tokens)
    heads_out = mixed.reshape(TOK_DEV, local_heads * DH)
    heads_all = ring_gather(heads_out, "head")
    groups = heads_all.shape[0]
    weight_rows = weight_rows.reshape(groups, -1, half)
    weight_other = weight_other.reshape(groups, -1, half)
    other_rank = 1 - core_rank
    bias_own = lax.dynamic_slice_in_dim(out_bias, core_rank * half, half, 0)
    bias_other = lax.dynamic_slice_in_dim(out_bias, other_rank * half, half, 0)
    own_cols = jnp.einsum(
        "gtk,gkc->tc", heads_all, weight_rows, preferred_element_type=jnp.float32
    ) + bias_own
    other_cols = jnp.einsum(
        "gtk,gkc->tc", heads_all, weight_other, preferred_element_type=jnp.float32
    ) + bias_other
    own_cols = own_cols.astype(jnp.bfloat16)
    other_cols = other_cols.astype(jnp.bfloat16)
    attended = jnp.where(
        core_rank == 0,
        jnp.concatenate([own_cols, other_cols], axis=1),
        jnp.concatenate([other_cols, own_cols], axis=1),
    )
    local_page = page_table - device_rank * BLK_DEV
    picker = (local_page[:, None] == jnp.arange(BLK_DEV, dtype=jnp.int32)[None, :]).astype(
        jnp.bfloat16
    )
    page_blocks = jnp.stack(
        [
            key_flat.reshape(BLK_DEV, PAGE, local_heads * DH),
            value_proj.reshape(BLK_DEV, PAGE, local_heads * DH),
        ],
        axis=1,
    )
    kv_pages = jnp.einsum(
        "bp,bctd->pctd", picker, page_blocks, preferred_element_type=jnp.float32
    ).astype(jnp.bfloat16)
    return (attended, kv_pages)


def solution(mesh):
    devices = mesh.devices
    cores = len({d.core_on_chip for d in devices.flat})
    columns = len({d.coords[0] for d in devices.flat})
    req_size, head_size = devices.shape
    split = Mesh(
        devices.reshape(req_size // (columns * cores), columns, cores, head_size),
        ("z", "x", "core", "head"),
    )
    placed = (
        P(REQ, "head"),
        P(REQ, "head"),
        P(REQ, "head"),
        P(),
        P(REQ),
        P(REQ, "head"),
        P("head"),
    )
    return jax.shard_map(
        local_body,
        mesh=split,
        in_specs=placed,
        out_specs=(P(REQ, "head"), P(REQ, None, None, "head")),
        check_vma=False,
    )
```

```python
import math

import jax
import jax.numpy as jnp
from jax import lax
from jax.sharding import Mesh, PartitionSpec as P


DH = 128
ROT = 32
PAGE = 128
BLK_DEV = 2
REACH = 4
TOK_DEV = 256


rope_base = 10000.0


REQ = ("z", "x", "core")


def passed_along(array, axis, by):
    count = lax.axis_size(axis)
    pairs = [(i, i + by) for i in range(count) if 0 <= i + by < count]
    return lax.ppermute(array, axis, pairs)


def ring_gather(piece, axis):
    count = lax.axis_size(axis)
    forward = [(i, (i + 1) % count) for i in range(count)]
    backward = [(i, (i - 1) % count) for i in range(count)]
    ahead = [piece]
    behind = []
    sent_ahead = piece
    sent_behind = piece
    for step in range(1, count // 2 + 1):
        sent_ahead = lax.ppermute(sent_ahead, axis, forward)
        behind.append(sent_ahead)
        if step < count - count // 2:
            sent_behind = lax.ppermute(sent_behind, axis, backward)
            ahead.append(sent_behind)
    relative = jnp.stack(ahead + behind[::-1], axis=0)
    return jnp.roll(relative, lax.axis_index(axis), axis=0)


def request_info(lengths, token_index):
    request_ends = jnp.cumsum(lengths) * PAGE
    request_starts = request_ends - lengths * PAGE
    inside = request_starts[None, :] <= token_index[:, None]
    request_id = jnp.sum(inside.astype(jnp.int32), axis=1) - 1
    opening = jnp.max(jnp.where(inside, request_starts[None, :], 0), axis=1)
    return (request_id, token_index - opening)


def rotate_heads(projected, position):
    values_f32 = projected.astype(jnp.float32)
    half_rot = ROT // 2
    frequency = jnp.exp(
        jnp.arange(half_rot, dtype=jnp.float32) * (-2.0 * math.log(rope_base) / ROT)
    )
    angles = position.astype(jnp.float32)[:, None] * frequency[None, :]
    cosine = jnp.cos(angles)[:, None, :]
    sine = jnp.sin(angles)[:, None, :]
    front_half = values_f32[..., :half_rot]
    back_half = values_f32[..., half_rot:ROT]
    turned = jnp.concatenate(
        [
            front_half * cosine - back_half * sine,
            back_half * cosine + front_half * sine,
            values_f32[..., ROT:],
        ],
        axis=-1,
    )
    return turned.astype(jnp.bfloat16)


def attend_block(query_rot, key_rot, value_rows, query_id, query_token, key_id, key_token):
    scores = jnp.einsum("qhd,khd->hqk", query_rot, key_rot, preferred_element_type=jnp.float32) * (
        1.0 / math.sqrt(DH)
    )
    allowed = (query_id[:, None] == key_id[None, :]) & (key_token[None, :] <= query_token[:, None])
    scores = jnp.where(allowed[None], scores, -jnp.inf)
    row_max = jnp.max(scores, axis=-1, keepdims=True)
    raised = jnp.exp(scores - row_max)
    probs = (raised / jnp.sum(raised, axis=-1, keepdims=True)).astype(jnp.bfloat16)
    mixed = jnp.einsum("hqk,khd->qhd", probs, value_rows, preferred_element_type=jnp.float32)
    return mixed.astype(jnp.bfloat16)


def local_body(query_proj, key_proj, value_proj, lengths, page_table, out_weight, out_bias):
    local_heads = query_proj.shape[1] // DH
    device_rank = lax.axis_index(REQ)
    core_rank = lax.axis_index("core")
    half = out_weight.shape[1] // 2
    weight_pair = lax.all_gather(out_weight, "core", axis=0, tiled=True)
    weight_rows = lax.dynamic_slice_in_dim(weight_pair, core_rank * half, half, 1)
    weight_rows = ring_gather(weight_rows, "x")
    weight_rows = weight_rows.reshape(-1, half)
    weight_rows, query_proj, key_proj = lax.optimization_barrier(
        (weight_rows, query_proj, key_proj)
    )
    weight_rows = lax.all_gather(weight_rows, "z", axis=0, tiled=True)
    weight_other = lax.ppermute(weight_rows, "core", [(0, 1), (1, 0)])
    first_token = device_rank * TOK_DEV
    own_tokens = first_token + jnp.arange(TOK_DEV, dtype=jnp.int32)
    request_id, position = request_info(lengths, own_tokens)
    query_rot = rotate_heads(query_proj.reshape(TOK_DEV, local_heads, DH), position)
    key_flat = rotate_heads(key_proj.reshape(TOK_DEV, local_heads, DH), position).reshape(
        TOK_DEV, local_heads * DH
    )
    halo = jnp.stack([key_flat, value_proj], axis=0)
    halo_list = [halo]
    for distance in range(1, REACH + 1):
        halo_list.append(passed_along(halo, REQ, distance))
    halo_stack = jnp.stack(halo_list[::-1], axis=1)
    key_stack = halo_stack[0]
    value_stack = halo_stack[1]
    key_rows = (REACH + 1) * TOK_DEV
    key_all = key_stack.reshape(key_rows, local_heads, DH)
    value_all = value_stack.reshape(key_rows, local_heads, DH)
    key_tokens = first_token - REACH * TOK_DEV + jnp.arange(key_rows, dtype=jnp.int32)
    key_id, _ = request_info(lengths, key_tokens)
    mixed = attend_block(query_rot, key_all, value_all, request_id, own_tokens, key_id, key_tokens)
    heads_out = mixed.reshape(TOK_DEV, local_heads * DH)
    heads_all = ring_gather(heads_out, "head")
    groups = heads_all.shape[0]
    weight_rows = weight_rows.reshape(groups, -1, half)
    weight_other = weight_other.reshape(groups, -1, half)
    other_rank = 1 - core_rank
    bias_own = lax.dynamic_slice_in_dim(out_bias, core_rank * half, half, 0)
    bias_other = lax.dynamic_slice_in_dim(out_bias, other_rank * half, half, 0)
    own_cols = jnp.einsum(
        "gtk,gkc->tc", heads_all, weight_rows, preferred_element_type=jnp.float32
    ) + bias_own
    other_cols = jnp.einsum(
        "gtk,gkc->tc", heads_all, weight_other, preferred_element_type=jnp.float32
    ) + bias_other
    own_cols = own_cols.astype(jnp.bfloat16)
    other_cols = other_cols.astype(jnp.bfloat16)
    attended = jnp.where(
        core_rank == 0,
        jnp.concatenate([own_cols, other_cols], axis=1),
        jnp.concatenate([other_cols, own_cols], axis=1),
    )
    local_page = page_table - device_rank * BLK_DEV
    picker = (local_page[:, None] == jnp.arange(BLK_DEV, dtype=jnp.int32)[None, :]).astype(
        jnp.bfloat16
    )
    page_blocks = jnp.stack(
        [
            key_flat.reshape(BLK_DEV, PAGE, local_heads * DH),
            value_proj.reshape(BLK_DEV, PAGE, local_heads * DH),
        ],
        axis=1,
    )
    kv_pages = jnp.einsum(
        "bp,bctd->pctd", picker, page_blocks, preferred_element_type=jnp.float32
    ).astype(jnp.bfloat16)
    return (attended, kv_pages)


def solution(mesh):
    devices = mesh.devices
    cores = len({d.core_on_chip for d in devices.flat})
    columns = len({d.coords[0] for d in devices.flat})
    req_size, head_size = devices.shape
    split = Mesh(
        devices.reshape(req_size // (columns * cores), columns, cores, head_size),
        ("z", "x", "core", "head"),
    )
    placed = (
        P(REQ, "head"),
        P(REQ, "head"),
        P(REQ, "head"),
        P(),
        P(REQ),
        P(REQ, "head"),
        P("head"),
    )
    return jax.shard_map(
        local_body,
        mesh=split,
        in_specs=placed,
        out_specs=(P(REQ, "head"), P(REQ, None, None, "head")),
        check_vma=False,
    )
```

```python
import math

import jax
import jax.numpy as jnp
from jax import lax
from jax.sharding import Mesh, PartitionSpec as P


DH = 128
ROT = 32
PAGE = 128
BLK_DEV = 2
REACH = 4
TOK_DEV = 256


rope_base = 10000.0


REQ = ("z", "x", "core")


def passed_along(array, axis, by):
    count = lax.axis_size(axis)
    pairs = [(i, i + by) for i in range(count) if 0 <= i + by < count]
    return lax.ppermute(array, axis, pairs)


def ring_gather(piece, axis):
    count = lax.axis_size(axis)
    forward = [(i, (i + 1) % count) for i in range(count)]
    backward = [(i, (i - 1) % count) for i in range(count)]
    ahead = [piece]
    behind = []
    sent_ahead = piece
    sent_behind = piece
    for step in range(1, count // 2 + 1):
        sent_ahead = lax.ppermute(sent_ahead, axis, forward)
        behind.append(sent_ahead)
        if step < count - count // 2:
            sent_behind = lax.ppermute(sent_behind, axis, backward)
            ahead.append(sent_behind)
    relative = jnp.stack(ahead + behind[::-1], axis=0)
    return jnp.roll(relative, lax.axis_index(axis), axis=0)


def request_info(lengths, token_index):
    request_ends = jnp.cumsum(lengths) * PAGE
    request_starts = request_ends - lengths * PAGE
    inside = request_starts[None, :] <= token_index[:, None]
    request_id = jnp.sum(inside.astype(jnp.int32), axis=1) - 1
    opening = jnp.max(jnp.where(inside, request_starts[None, :], 0), axis=1)
    return (request_id, token_index - opening)


def rotate_heads(projected, position):
    values_f32 = projected.astype(jnp.float32)
    half_rot = ROT // 2
    frequency = jnp.exp(
        jnp.arange(half_rot, dtype=jnp.float32) * (-2.0 * math.log(rope_base) / ROT)
    )
    angles = position.astype(jnp.float32)[:, None] * frequency[None, :]
    cosine = jnp.cos(angles)[:, None, :]
    sine = jnp.sin(angles)[:, None, :]
    front_half = values_f32[..., :half_rot]
    back_half = values_f32[..., half_rot:ROT]
    turned = jnp.concatenate(
        [
            front_half * cosine - back_half * sine,
            back_half * cosine + front_half * sine,
            values_f32[..., ROT:],
        ],
        axis=-1,
    )
    return turned.astype(jnp.bfloat16)


def attend_heads(query_rot, key_rot, value_rows, query_id, query_token, key_id, key_token):
    allowed = (query_id[:, None] == key_id[None, :]) & (key_token[None, :] <= query_token[:, None])
    outputs = []
    for head in range(query_rot.shape[1] // DH):
        columns = slice(head * DH, (head + 1) * DH)
        scores = jnp.dot(
            query_rot[:, columns], key_rot[:, columns].T, preferred_element_type=jnp.float32
        ) * (1.0 / math.sqrt(DH))
        scores = jnp.where(allowed, scores, -jnp.inf)
        row_max = jnp.max(scores, axis=-1, keepdims=True)
        raised = jnp.exp(scores - row_max)
        probs = (raised / jnp.sum(raised, axis=-1, keepdims=True)).astype(jnp.bfloat16)
        mixed = jnp.dot(probs, value_rows[:, columns], preferred_element_type=jnp.float32)
        outputs.append(mixed.astype(jnp.bfloat16))
    return jnp.concatenate(outputs, axis=1)


def local_body(query_proj, key_proj, value_proj, lengths, page_table, out_weight, out_bias):
    local_heads = query_proj.shape[1] // DH
    device_rank = lax.axis_index(REQ)
    core_rank = lax.axis_index("core")
    half = out_weight.shape[1] // 2
    weight_pair = lax.all_gather(out_weight, "core", axis=0, tiled=True)
    weight_rows = lax.dynamic_slice_in_dim(weight_pair, core_rank * half, half, 1)
    weight_rows = lax.all_gather(weight_rows, "x", axis=0, tiled=True)
    weight_rows, query_proj, key_proj = lax.optimization_barrier(
        (weight_rows, query_proj, key_proj)
    )
    weight_rows = lax.all_gather(weight_rows, "z", axis=0, tiled=True)
    weight_other = lax.ppermute(weight_rows, "core", [(0, 1), (1, 0)])
    first_token = device_rank * TOK_DEV
    own_tokens = first_token + jnp.arange(TOK_DEV, dtype=jnp.int32)
    request_id, position = request_info(lengths, own_tokens)
    query_rot = rotate_heads(query_proj.reshape(TOK_DEV, local_heads, DH), position)
    key_flat = rotate_heads(key_proj.reshape(TOK_DEV, local_heads, DH), position).reshape(
        TOK_DEV, local_heads * DH
    )
    halo = jnp.stack([key_flat, value_proj], axis=0)
    halo_list = [halo]
    for distance in range(1, REACH + 1):
        halo_list.append(passed_along(halo, REQ, distance))
    key_all = jnp.concatenate([part[0] for part in halo_list[::-1]], axis=0)
    value_all = jnp.concatenate([part[1] for part in halo_list[::-1]], axis=0)
    key_rows = (REACH + 1) * TOK_DEV
    key_tokens = first_token - REACH * TOK_DEV + jnp.arange(key_rows, dtype=jnp.int32)
    key_id, _ = request_info(lengths, key_tokens)
    heads_out = attend_heads(
        query_rot.reshape(TOK_DEV, local_heads * DH),
        key_all,
        value_all,
        request_id,
        own_tokens,
        key_id,
        key_tokens,
    )
    heads_all = ring_gather(heads_out, "head")
    groups = heads_all.shape[0]
    weight_rows = weight_rows.reshape(groups, -1, half)
    weight_other = weight_other.reshape(groups, -1, half)
    other_rank = 1 - core_rank
    bias_own = lax.dynamic_slice_in_dim(out_bias, core_rank * half, half, 0)
    bias_other = lax.dynamic_slice_in_dim(out_bias, other_rank * half, half, 0)
    own_cols = jnp.einsum(
        "gtk,gkc->tc", heads_all, weight_rows, preferred_element_type=jnp.float32
    ) + bias_own
    other_cols = jnp.einsum(
        "gtk,gkc->tc", heads_all, weight_other, preferred_element_type=jnp.float32
    ) + bias_other
    own_cols = own_cols.astype(jnp.bfloat16)
    other_cols = other_cols.astype(jnp.bfloat16)
    attended = jnp.where(
        core_rank == 0,
        jnp.concatenate([own_cols, other_cols], axis=1),
        jnp.concatenate([other_cols, own_cols], axis=1),
    )
    local_page = page_table - device_rank * BLK_DEV
    picker = (local_page[:, None] == jnp.arange(BLK_DEV, dtype=jnp.int32)[None, :]).astype(
        jnp.bfloat16
    )
    page_blocks = jnp.stack(
        [
            key_flat.reshape(BLK_DEV, PAGE, local_heads * DH),
            value_proj.reshape(BLK_DEV, PAGE, local_heads * DH),
        ],
        axis=1,
    )
    kv_pages = jnp.einsum(
        "bp,bctd->pctd", picker, page_blocks, preferred_element_type=jnp.float32
    ).astype(jnp.bfloat16)
    return (attended, kv_pages)


def solution(mesh):
    devices = mesh.devices
    cores = len({d.core_on_chip for d in devices.flat})
    columns = len({d.coords[0] for d in devices.flat})
    req_size, head_size = devices.shape
    split = Mesh(
        devices.reshape(req_size // (columns * cores), columns, cores, head_size),
        ("z", "x", "core", "head"),
    )
    placed = (
        P(REQ, "head"),
        P(REQ, "head"),
        P(REQ, "head"),
        P(),
        P(REQ),
        P(REQ, "head"),
        P("head"),
    )
    return jax.shard_map(
        local_body,
        mesh=split,
        in_specs=placed,
        out_specs=(P(REQ, "head"), P(REQ, None, None, "head")),
        check_vma=False,
    )
```

```python
import math

import jax
import jax.numpy as jnp
from jax import lax
from jax.sharding import Mesh, PartitionSpec as P


DH = 128
ROT = 32
PAGE = 128
BLK_DEV = 2
REACH = 4
TOK_DEV = 256


rope_base = 10000.0


REQ = ("z", "x", "core")


def passed_along(array, axis, by):
    count = lax.axis_size(axis)
    pairs = [(i, i + by) for i in range(count) if 0 <= i + by < count]
    return lax.ppermute(array, axis, pairs)


def ring_gather(piece, axis):
    count = lax.axis_size(axis)
    forward = [(i, (i + 1) % count) for i in range(count)]
    backward = [(i, (i - 1) % count) for i in range(count)]
    ahead = [piece]
    behind = []
    sent_ahead = piece
    sent_behind = piece
    for step in range(1, count // 2 + 1):
        sent_ahead = lax.ppermute(sent_ahead, axis, forward)
        behind.append(sent_ahead)
        if step < count - count // 2:
            sent_behind = lax.ppermute(sent_behind, axis, backward)
            ahead.append(sent_behind)
    relative = jnp.stack(ahead + behind[::-1], axis=0)
    return jnp.roll(relative, lax.axis_index(axis), axis=0)


def direct_gather(piece, axis):
    count = lax.axis_size(axis)
    relative = [piece]
    for distance in range(1, count):
        pairs = [(i, (i - distance) % count) for i in range(count)]
        relative.append(lax.ppermute(piece, axis, pairs))
    return jnp.roll(jnp.stack(relative, axis=0), lax.axis_index(axis), axis=0)


def request_info(lengths, token_index):
    request_ends = jnp.cumsum(lengths) * PAGE
    request_starts = request_ends - lengths * PAGE
    inside = request_starts[None, :] <= token_index[:, None]
    request_id = jnp.sum(inside.astype(jnp.int32), axis=1) - 1
    opening = jnp.max(jnp.where(inside, request_starts[None, :], 0), axis=1)
    return (request_id, token_index - opening)


def rotate_heads(projected, position):
    values_f32 = projected.astype(jnp.float32)
    half_rot = ROT // 2
    frequency = jnp.exp(
        jnp.arange(half_rot, dtype=jnp.float32) * (-2.0 * math.log(rope_base) / ROT)
    )
    angles = position.astype(jnp.float32)[:, None] * frequency[None, :]
    cosine = jnp.cos(angles)[:, None, :]
    sine = jnp.sin(angles)[:, None, :]
    front_half = values_f32[..., :half_rot]
    back_half = values_f32[..., half_rot:ROT]
    turned = jnp.concatenate(
        [
            front_half * cosine - back_half * sine,
            back_half * cosine + front_half * sine,
            values_f32[..., ROT:],
        ],
        axis=-1,
    )
    return turned.astype(jnp.bfloat16)


def attend_heads(query_rot, key_rot, value_rows, query_id, query_token, key_id, key_token):
    allowed = (query_id[:, None] == key_id[None, :]) & (key_token[None, :] <= query_token[:, None])
    outputs = []
    for head in range(query_rot.shape[1] // DH):
        columns = slice(head * DH, (head + 1) * DH)
        scores = jnp.dot(
            query_rot[:, columns], key_rot[:, columns].T, preferred_element_type=jnp.float32
        ) * (1.0 / math.sqrt(DH))
        scores = jnp.where(allowed, scores, -jnp.inf)
        row_max = jnp.max(scores, axis=-1, keepdims=True)
        raised = jnp.exp(scores - row_max)
        probs = (raised / jnp.sum(raised, axis=-1, keepdims=True)).astype(jnp.bfloat16)
        mixed = jnp.dot(probs, value_rows[:, columns], preferred_element_type=jnp.float32)
        outputs.append(mixed.astype(jnp.bfloat16))
    return jnp.concatenate(outputs, axis=1)


def local_body(query_proj, key_proj, value_proj, lengths, page_table, out_weight, out_bias):
    local_heads = query_proj.shape[1] // DH
    device_rank = lax.axis_index(REQ)
    core_rank = lax.axis_index("core")
    half = out_weight.shape[1] // 2
    weight_pair = lax.all_gather(out_weight, "core", axis=0, tiled=True)
    weight_rows = lax.dynamic_slice_in_dim(weight_pair, core_rank * half, half, 1)
    weight_rows = direct_gather(weight_rows, "x")
    weight_rows = weight_rows.reshape(-1, half)
    weight_rows, query_proj, key_proj = lax.optimization_barrier(
        (weight_rows, query_proj, key_proj)
    )
    weight_rows = lax.all_gather(weight_rows, "z", axis=0, tiled=True)
    weight_other = lax.ppermute(weight_rows, "core", [(0, 1), (1, 0)])
    first_token = device_rank * TOK_DEV
    own_tokens = first_token + jnp.arange(TOK_DEV, dtype=jnp.int32)
    request_id, position = request_info(lengths, own_tokens)
    query_rot = rotate_heads(query_proj.reshape(TOK_DEV, local_heads, DH), position)
    key_flat = rotate_heads(key_proj.reshape(TOK_DEV, local_heads, DH), position).reshape(
        TOK_DEV, local_heads * DH
    )
    halo = jnp.stack([key_flat, value_proj], axis=0)
    halo_list = [halo]
    for distance in range(1, REACH + 1):
        halo_list.append(passed_along(halo, REQ, distance))
    key_all = jnp.concatenate([part[0] for part in halo_list[::-1]], axis=0)
    value_all = jnp.concatenate([part[1] for part in halo_list[::-1]], axis=0)
    key_rows = (REACH + 1) * TOK_DEV
    key_tokens = first_token - REACH * TOK_DEV + jnp.arange(key_rows, dtype=jnp.int32)
    key_id, _ = request_info(lengths, key_tokens)
    heads_out = attend_heads(
        query_rot.reshape(TOK_DEV, local_heads * DH),
        key_all,
        value_all,
        request_id,
        own_tokens,
        key_id,
        key_tokens,
    )
    heads_all = ring_gather(heads_out, "head")
    groups = heads_all.shape[0]
    weight_rows = weight_rows.reshape(groups, -1, half)
    weight_other = weight_other.reshape(groups, -1, half)
    other_rank = 1 - core_rank
    bias_own = lax.dynamic_slice_in_dim(out_bias, core_rank * half, half, 0)
    bias_other = lax.dynamic_slice_in_dim(out_bias, other_rank * half, half, 0)
    own_cols = jnp.einsum(
        "gtk,gkc->tc", heads_all, weight_rows, preferred_element_type=jnp.float32
    ) + bias_own
    other_cols = jnp.einsum(
        "gtk,gkc->tc", heads_all, weight_other, preferred_element_type=jnp.float32
    ) + bias_other
    own_cols = own_cols.astype(jnp.bfloat16)
    other_cols = other_cols.astype(jnp.bfloat16)
    attended = jnp.where(
        core_rank == 0,
        jnp.concatenate([own_cols, other_cols], axis=1),
        jnp.concatenate([other_cols, own_cols], axis=1),
    )
    local_page = page_table - device_rank * BLK_DEV
    picker = (local_page[:, None] == jnp.arange(BLK_DEV, dtype=jnp.int32)[None, :]).astype(
        jnp.bfloat16
    )
    page_blocks = jnp.stack(
        [
            key_flat.reshape(BLK_DEV, PAGE, local_heads * DH),
            value_proj.reshape(BLK_DEV, PAGE, local_heads * DH),
        ],
        axis=1,
    )
    kv_pages = jnp.einsum(
        "bp,bctd->pctd", picker, page_blocks, preferred_element_type=jnp.float32
    ).astype(jnp.bfloat16)
    return (attended, kv_pages)


def solution(mesh):
    devices = mesh.devices
    cores = len({d.core_on_chip for d in devices.flat})
    columns = len({d.coords[0] for d in devices.flat})
    req_size, head_size = devices.shape
    split = Mesh(
        devices.reshape(req_size // (columns * cores), columns, cores, head_size),
        ("z", "x", "core", "head"),
    )
    placed = (
        P(REQ, "head"),
        P(REQ, "head"),
        P(REQ, "head"),
        P(),
        P(REQ),
        P(REQ, "head"),
        P("head"),
    )
    return jax.shard_map(
        local_body,
        mesh=split,
        in_specs=placed,
        out_specs=(P(REQ, "head"), P(REQ, None, None, "head")),
        check_vma=False,
    )
```
